128 devices in a mesh: row: 8 (over z_lo, y), col: 16 (over x, z_hi, core).
Axes of the slice: x: 4, y: 4, z: 4 (z_hi: 2, z_lo: 2; z = z_hi * 2 + z_lo), core: 2. Of those that a mesh axis runs over, the one named last changes fastest.
Arguments:
- tokens: bfloat16 [2048, 2304], P('row', 'col'), may hold values from -6 to 6
- gate_weight: bfloat16 [8, 2304, 5760], P(None, 'col', 'row'), may hold values from -0.125 to 0.125
- up_weight: bfloat16 [8, 2304, 5760], P(None, 'col', 'row'), may hold values from -0.125 to 0.125
- down_weight: bfloat16 [8, 5760, 2304], P(None, 'row', 'col'), may hold values from -0.078125 to 0.078125
- route_ids: int32 [2048, 2], replicated, may hold values from 0 to 7, all different within a row; in each aligned block of 2048 rows (0 to 2047, 2048 to 4095, ...) at most 1024 rows name the same one
- route_weight: float32 [2048, 2], replicated, may hold values from 0.2 to 1
- prefill_cache: bfloat16 [2, 2048, 16, 2304], P(None, ('row', 'col')), may hold values from -6 to 6
- dest_col: int32 [8, 16, 16], P('row'), may hold values from 0 to 15, as said below
- dest_slot: int32 [8, 16, 16], P('row'), may hold values from 0 to 15, as said below
- pages_used: int32 [8, 16], P('row'), may hold values from 4 to 16, as said below
Outputs:
- mixed: bfloat16 [2048, 2304], P('row', 'col')
- decode_cache: bfloat16 [2, 2048, 16, 2304], P(None, ('row', 'col'))
The draws below stay inside these ranges and needn't reach their ends.
Inputs may be any that keep to these rules, and one draw needn't show every extreme that they name: `route_ids`: each token names two different experts; no expert is named by more than 1024 tokens, a bound that some block reaches. For every device (r, c), dest_col[r, c, :] names each col index exactly 1 times. For every r and col index c2, the page slots of row r with dest_col = c2 carry distinct dest_slot values, so they fill all 16 slots of device (r, c2). The live slots of a device are its first pages_used slots; some device has all 16 live.
All inputs are finite; a program needn't handle non-finite values.
Results may differ from the reference program's by a relative error of at most 0.03.
Values may be sent and summed in bfloat16 or wider, within the bound.
No kernel may reach another device: no remote copies, remote signals or barrier semaphores. Data moves between devices by JAX's collectives and lax.ppermute only.
A program may use at most 192 MiB of HBM per device.

```python
import math
import jax
import jax.numpy as jnp
import numpy as np
from jax import lax

D = 2304
FF = 5760
EXPERTS = 8
HEADS = 36
HEAD_DIM = 64
PAGE = 16
PEER = 1
TOKENS = 2048
CAP = 1024
SLOTS = 16
N_ROW = 8
N_COL = 16


def one_permutation(sub_key):
    return jax.random.permutation(sub_key, SLOTS).astype(jnp.int32)


def page_plan(key):
    device_count = N_ROW * N_COL
    send_keys = jax.random.split(jax.random.fold_in(key, 11), device_count)
    recv_keys = jax.random.split(jax.random.fold_in(key, 23), device_count)
    send_perm = jax.vmap(one_permutation)(send_keys).reshape(N_ROW, N_COL, SLOTS)
    recv_perm = jax.vmap(one_permutation)(recv_keys).reshape(N_ROW, N_COL, SLOTS)
    dest_index = send_perm // PEER
    arrival = jnp.arange(N_COL, dtype=jnp.int32)[None, :, None] * PEER + send_perm % PEER
    row_index = jnp.arange(N_ROW, dtype=jnp.int32)[:, None, None]
    slot_table = recv_perm[row_index, dest_index, arrival]
    return (dest_index.astype(jnp.int32), slot_table.astype(jnp.int32))


def draw_dest_col(key, part):
    return page_plan(key)[0]


def draw_dest_slot(key, part):
    return page_plan(key)[1]


def draw_pages_used(key, part):
    keys = jax.random.split(jax.random.fold_in(key, 37), 3)
    halving = jax.random.randint(keys[0], (N_ROW, N_COL), 0, 3)
    base_count = jnp.right_shift(jnp.full((N_ROW, N_COL), SLOTS, jnp.int32), halving)
    extra_count = jax.random.randint(keys[1], (N_ROW, N_COL), 0, SLOTS // 8 + 1)
    used_count = jnp.minimum(base_count + extra_count, SLOTS).reshape(-1)
    full_device = jax.random.randint(keys[2], (), 0, N_ROW * N_COL)
    used_count = jnp.where(jnp.arange(N_ROW * N_COL) == full_device, SLOTS, used_count)
    return used_count.reshape(N_ROW, N_COL).astype(jnp.int32)


def block_scale(key, shape, cuts, smallest, high):
    level, own = 1.0, jax.random.fold_in(key, 6)
    for axis_at, blocks in cuts:
        draws = jnp.exp(jax.random.uniform(jax.random.fold_in(own, axis_at), (blocks,), jnp.float32, smallest / len(cuts), high / len(cuts)))
        level = level * jnp.repeat(draws, shape[axis_at] // blocks).reshape([-1 if axis == axis_at else 1 for axis in range(len(shape))])
    return level


def deal_out(stream_key, own, number, rows, amount, top, most, skew):
    sequence = jax.random.permutation(stream_key, amount)
    heavy_load, usual = shares(amount, rows * top, most, skew, True), shares(amount, rows * top, most, skew, False)
    places = jnp.arange(amount)

    def named(tallies, turn):
        used = int((tallies > 0).sum())
        fixed = max(1, used // 4)
        passed = fixed + (places - fixed + turn * (used - fixed)) % max(1, amount - fixed)
        return jnp.zeros((amount,), jnp.int32).at[sequence[jnp.where(places < fixed, places, passed)]].set(jnp.asarray(tallies, jnp.int32))

    tallies = jnp.where(number % 4 == 0, named(heavy_load, number // 4), named(usual, number - number // 4 - 1))
    mixed = jax.random.permutation(jax.random.fold_in(own, 3), amount)
    source_of, taker = mixed[0:amount // 2 * 2:2], mixed[1:amount // 2 * 2:2]
    margin = jnp.minimum(tallies[source_of] - 1, most - tallies[taker]) // 2
    margin = jnp.where((source_of == sequence[0]) | (taker == sequence[0]) | (tallies[taker] == 0), 0, jnp.maximum(margin, 0))
    passed = jax.random.randint(jax.random.fold_in(own, 4), (amount // 2,), 0, 1 << 20) % (margin + 1)
    tallies = tallies.at[source_of].add(-passed).at[taker].add(passed)
    members = jnp.searchsorted(jnp.cumsum(tallies), jnp.arange(rows * top), side="right").astype(jnp.int32)
    listing = members.reshape(top, rows).T
    listing = listing[jax.random.permutation(jax.random.fold_in(own, 1), rows)]
    turn = jax.random.randint(jax.random.fold_in(own, 2), (rows, 1), 0, top)
    return jnp.take_along_axis(listing, (jnp.arange(top)[None, :] + turn) % top, axis=1)


def shares(count, total, limit, skew, full):
    loads = [(1 << 20) // math.isqrt(standing ** skew) + 1 for standing in range(1, count + 1)]
    largest = limit if full else min(limit, max(-(-total // count), total * loads[0] // sum(loads)))
    least = 1 if total - largest >= count - 1 else 0
    holding, spare = [largest] + [least] * (count - 1), total - largest - least * (count - 1)
    while spare > 0:
        movable = [i for i in range(1, count) if holding[i] < largest] or [i for i in range(1, count) if holding[i] < limit]
        mass, left = sum([loads[i] for i in movable]), spare
        for i in movable:
            addition = min(limit - holding[i], max(1, left * loads[i] // mass), spare)
            holding[i] = holding[i] + addition
            spare = spare - addition
    return np.array(holding)


def scatter_about(key, dims, scale, bound, cuts=(), held_as=jnp.bfloat16):
    entries = scale * jax.random.normal(key, dims, jnp.float32)
    if cuts:
        entries = entries * block_scale(key, dims, cuts, -0.22, 0.18)
    return jnp.clip(entries, -bound, bound).astype(held_as)


def setup_inputs(seed: int = 0) -> dict:
    splits = jax.random.split(jax.random.key(seed), 11)
    tokens = scatter_about(splits[0], (TOKENS, D), 1.0, 6.0, ((0, 8), (1, 16)))
    gate_weight = scatter_about(splits[1], (EXPERTS, D, FF), D ** -0.5, 0.125, ((1, 16), (2, 8)))
    up_weight = scatter_about(splits[2], (EXPERTS, D, FF), D ** -0.5, 0.125, ((1, 16), (2, 8)))
    down_weight = scatter_about(splits[3], (EXPERTS, FF, D), FF ** -0.5, 0.078125, ((1, 8), (2, 16)))
    route_ids_keys = jax.random.split(jax.random.fold_in(splits[4], 1), TOKENS // TOKENS)
    route_ids_turns = jax.random.permutation(jax.random.fold_in(splits[4], 3), TOKENS // TOKENS)
    route_ids = jax.vmap(lambda own, number: deal_out(jax.random.fold_in(splits[4], 2), own, number, TOKENS, EXPERTS, 2, CAP, 1))(route_ids_keys, route_ids_turns).reshape((TOKENS, 2))
    route_weight = jnp.clip(jax.random.uniform(splits[5], (TOKENS, 2), jnp.float32, 0.2, 1.0), 0.2, 1.0)
    prefill_cache = scatter_about(splits[6], (2, N_ROW * N_COL * SLOTS, PAGE, HEADS * HEAD_DIM), 1.0, 6.0, ((1, 128),))
    dest_col = draw_dest_col(jax.random.fold_in(splits[10], 71), 0)
    dest_slot = draw_dest_slot(jax.random.fold_in(splits[10], 71), 0)
    pages_used = draw_pages_used(jax.random.fold_in(splits[10], 71), 0)
    return dict(tokens=tokens, gate_weight=gate_weight, up_weight=up_weight, down_weight=down_weight, route_ids=route_ids, route_weight=route_weight, prefill_cache=prefill_cache, dest_col=dest_col, dest_slot=dest_slot, pages_used=pages_used)


def expert_order(route_ids):
    flat_expert = route_ids.reshape(-1).astype(jnp.int32)
    sort_order = jnp.argsort(flat_expert, stable=True).astype(jnp.int32)
    labels = jnp.arange(EXPERTS, dtype=jnp.int32)
    below = jnp.sum((flat_expert[None, :] < labels[:, None]).astype(jnp.int32), axis=1)
    starts = jnp.minimum(below, flat_expert.shape[0] - CAP)
    return sort_order, flat_expert[sort_order], starts


def reference(tokens, gate_weight, up_weight, down_weight, route_ids, route_weight, prefill_cache, dest_col, dest_slot, pages_used):
    sort_order, row_expert, starts = expert_order(route_ids)
    row_token = sort_order // 2
    slot_rows = tokens[row_token]
    row_weight = route_weight.reshape(-1)[sort_order]
    assignments = slot_rows.shape[0]
    block_width = D // N_COL
    totals = jnp.zeros((assignments, D), jnp.float32)
    for expert in range(EXPERTS):
        window_start = starts[expert]
        window = lax.dynamic_slice_in_dim(slot_rows, window_start, CAP, 0)
        paired = jnp.concatenate([gate_weight[expert], up_weight[expert]], axis=1)
        summed = jnp.zeros((CAP, 2 * FF), jnp.float32)
        for block_index in range(N_COL):
            lower = block_index * block_width
            upper = lower + block_width
            part_sum = jnp.dot(window[:, lower:upper], paired[lower:upper], preferred_element_type=jnp.float32)
            rounded = lax.optimization_barrier(part_sum.astype(jnp.bfloat16))
            summed = summed + rounded.astype(jnp.float32)
        gate_part = summed[:, :FF]
        up_part = summed[:, FF:]
        weight_window = lax.dynamic_slice_in_dim(row_weight, window_start, CAP, 0)
        hidden = (weight_window[:, None] * jax.nn.silu(gate_part) * up_part).astype(jnp.bfloat16)
        down_rows = jnp.dot(hidden, down_weight[expert], preferred_element_type=jnp.float32)
        is_owner = lax.dynamic_slice_in_dim(row_expert, window_start, CAP, 0) == expert
        current = lax.dynamic_slice_in_dim(totals, window_start, CAP, 0)
        totals = lax.dynamic_update_slice_in_dim(totals, jnp.where(is_owner[:, None], down_rows, current), window_start, 0)
    mixed = jnp.zeros((TOKENS, D), jnp.float32).at[row_token].add(totals).astype(jnp.bfloat16)

    cache_width = prefill_cache.shape[3]
    page_index = jnp.arange(SLOTS, dtype=jnp.int32)
    is_live = page_index[None, None, :] < pages_used[:, :, None]
    source_pages = prefill_cache.reshape(2, N_ROW, N_COL, SLOTS, PAGE, cache_width)
    masked = jnp.where(is_live[None, :, :, :, None, None], source_pages, jnp.zeros((), prefill_cache.dtype))
    masked = masked.reshape(prefill_cache.shape)
    row_base = jnp.arange(N_ROW, dtype=jnp.int32)[:, None, None] * N_COL
    target = ((row_base + dest_col) * SLOTS + dest_slot).reshape(-1).astype(jnp.int32)
    decode_cache = jnp.zeros_like(prefill_cache).at[:, target].set(masked)
    return mixed, decode_cache
```

```python
import jax
import jax.numpy as jnp
from jax import lax
from jax.sharding import PartitionSpec as P


def move_pages(prefill_cache, dest_col, dest_slot, pages_used):
    col_devices = lax.axis_size("col")
    own_index = lax.axis_index("col")
    slot_count = prefill_cache.shape[1]
    per_peer = slot_count // col_devices
    dest_table = dest_col[0]
    targets = dest_slot[0]
    page_index = jnp.arange(slot_count, dtype=jnp.int32)
    same_dest = dest_table[:, :, None] == dest_table[:, None, :]
    earlier = page_index[None, :] < page_index[:, None]
    dest_rank = jnp.sum((same_dest & earlier[None]).astype(jnp.int32), axis=2)
    send_order = lax.dynamic_index_in_dim(
        dest_table * per_peer + dest_rank, own_index, 0, keepdims=False
    )
    inverse = jnp.zeros((slot_count,), jnp.int32).at[send_order].set(page_index)
    own_used = lax.dynamic_index_in_dim(pages_used[0], own_index, 0, keepdims=False)
    is_live = page_index < own_used
    masked_pages = jnp.where(
        is_live[None, :, None, None], prefill_cache, jnp.zeros((), prefill_cache.dtype)
    )
    received = lax.all_to_all(
        masked_pages[:, inverse], "col", split_axis=1, concat_axis=1, tiled=True
    )
    senders = jnp.arange(col_devices, dtype=jnp.int32)[:, None]
    arrival = jnp.where(dest_table == own_index, senders * per_peer + dest_rank, slot_count)
    slot_of_arrival = (
        jnp.zeros((slot_count + 1,), jnp.int32)
        .at[arrival.reshape(-1)]
        .set(targets.reshape(-1))[:slot_count]
    )
    source_of_slot = jnp.zeros((slot_count,), jnp.int32).at[slot_of_arrival].set(page_index)
    return received[:, source_of_slot]


def shards(
    tokens,
    gate_weight,
    up_weight,
    down_weight,
    route_ids,
    route_weight,
    prefill_cache,
    dest_col,
    dest_slot,
    pages_used,
):
    decode_cache = move_pages(prefill_cache, dest_col, dest_slot, pages_used)
    gathered = lax.all_gather(tokens, "row", axis=0, tiled=True)
    token_count, width = gathered.shape
    experts = gate_weight.shape[0]
    hidden_width = gate_weight.shape[2]
    labels = jnp.arange(experts, dtype=jnp.int32)
    onehot = route_ids[:, :, None] == labels[None, None, :]
    expanded = jnp.where(
        onehot[:, :, :, None], gathered[:, None, None, :], jnp.zeros((), gathered.dtype)
    ).reshape(token_count * 2, experts * width)
    paired = jnp.concatenate([gate_weight, up_weight], axis=2).reshape(
        experts * width, 2 * hidden_width
    )
    partial_sums = jnp.dot(expanded, paired, preferred_element_type=jnp.float32)
    summed = lax.psum_scatter(
        partial_sums.astype(jnp.bfloat16), "col", scatter_dimension=0, tiled=True
    ).astype(jnp.float32)
    share_rows = summed.shape[0]
    own_weight = lax.dynamic_slice_in_dim(
        route_weight.reshape(-1), lax.axis_index("col") * share_rows, share_rows, 0
    )
    hidden = (
        own_weight[:, None] * jax.nn.silu(summed[:, :hidden_width]) * summed[:, hidden_width:]
    ).astype(jnp.bfloat16)
    hidden_all = lax.all_gather(hidden, "col", axis=0, tiled=True).reshape(
        token_count, 2, 1, hidden_width
    )
    picked = jnp.where(onehot[:, :, :, None], hidden_all, jnp.zeros((), hidden_all.dtype))
    by_expert = jnp.sum(picked, axis=1).reshape(token_count, experts * hidden_width)
    down_flat = down_weight.reshape(experts * hidden_width, down_weight.shape[2])
    per_token = jnp.dot(by_expert, down_flat, preferred_element_type=jnp.float32)
    mixed = lax.psum_scatter(per_token.astype(jnp.bfloat16), "row", scatter_dimension=0, tiled=True)
    return (mixed, decode_cache)


def solution(mesh):
    in_specs = (
        P("row", "col"),
        P(None, "col", "row"),
        P(None, "col", "row"),
        P(None, "row", "col"),
        P(),
        P(),
        P(None, ("row", "col"), None, None),
        P("row", None, None),
        P("row", None, None),
        P("row", None),
    )
    out_specs = (P("row", "col"), P(None, ("row", "col"), None, None))
    return jax.shard_map(shards, mesh=mesh, in_specs=in_specs, out_specs=out_specs, check_vma=False)
```

```python
import jax
import jax.numpy as jnp
from jax import lax
from jax.sharding import PartitionSpec as P
from jax.experimental import pallas as pl


def move_pages(prefill_cache, dest_col, dest_slot, pages_used):
    col_devices = lax.axis_size("col")
    own_index = lax.axis_index("col")
    slot_count = prefill_cache.shape[1]
    per_peer = slot_count // col_devices
    dest_table = dest_col[0]
    targets = dest_slot[0]
    page_index = jnp.arange(slot_count, dtype=jnp.int32)
    same_dest = dest_table[:, :, None] == dest_table[:, None, :]
    earlier = page_index[None, :] < page_index[:, None]
    dest_rank = jnp.sum((same_dest & earlier[None]).astype(jnp.int32), axis=2)
    send_order = lax.dynamic_index_in_dim(
        dest_table * per_peer + dest_rank, own_index, 0, keepdims=False
    )
    inverse = jnp.zeros((slot_count,), jnp.int32).at[send_order].set(page_index)
    own_used = lax.dynamic_index_in_dim(pages_used[0], own_index, 0, keepdims=False)
    is_live = page_index < own_used
    masked_pages = jnp.where(
        is_live[None, :, None, None], prefill_cache, jnp.zeros((), prefill_cache.dtype)
    )
    received = lax.all_to_all(
        masked_pages[:, inverse], "col", split_axis=1, concat_axis=1, tiled=True
    )
    senders = jnp.arange(col_devices, dtype=jnp.int32)[:, None]
    arrival = jnp.where(dest_table == own_index, senders * per_peer + dest_rank, slot_count)
    slot_of_arrival = (
        jnp.zeros((slot_count + 1,), jnp.int32)
        .at[arrival.reshape(-1)]
        .set(targets.reshape(-1))[:slot_count]
    )
    source_of_slot = jnp.zeros((slot_count,), jnp.int32).at[slot_of_arrival].set(page_index)
    return received[:, source_of_slot]


def gate_up_kernel(ids_ref, x_ref, g_ref, u_ref, go_ref, uo_ref):
    x = x_ref[...]
    ids = ids_ref[...]
    zero = jnp.zeros_like(x)
    rows = x.shape[0]
    width = g_ref.shape[2]
    acc_g = jnp.zeros((2 * rows, width), jnp.float32)
    acc_u = jnp.zeros((2 * rows, width), jnp.float32)
    for e in range(g_ref.shape[0]):
        lhs = jnp.concatenate(
            [jnp.where(ids[:, 0:1] == e, x, zero), jnp.where(ids[:, 1:2] == e, x, zero)], axis=0
        )
        acc_g = acc_g + jnp.dot(lhs, g_ref[e], preferred_element_type=jnp.float32)
        acc_u = acc_u + jnp.dot(lhs, u_ref[e], preferred_element_type=jnp.float32)
    go_ref[...] = acc_g.astype(go_ref.dtype).reshape(go_ref.shape)
    uo_ref[...] = acc_u.astype(uo_ref.dtype).reshape(uo_ref.shape)


def down_kernel(ids_ref, h_ref, d_ref, o_ref):
    ids = ids_ref[...]
    first = h_ref[0]
    second = h_ref[1]
    zero = jnp.zeros_like(first)
    acc = jnp.zeros(o_ref.shape, jnp.float32)
    for e in range(d_ref.shape[0]):
        lhs = jnp.where(ids[:, 0:1] == e, first, jnp.where(ids[:, 1:2] == e, second, zero))
        acc = acc + jnp.dot(lhs, d_ref[e], preferred_element_type=jnp.float32)
    o_ref[...] = acc.astype(o_ref.dtype)


def gate_up(route_ids, gathered, gate_weight, up_weight, tile):
    token_count, width = gathered.shape
    experts, _, hidden_width = gate_weight.shape
    out = jax.ShapeDtypeStruct((2, token_count, hidden_width), jnp.bfloat16)
    weight_spec = pl.BlockSpec((experts, width, hidden_width), lambda i: (0, 0, 0))
    out_spec = pl.BlockSpec((2, tile, hidden_width), lambda i: (0, i, 0))
    return pl.pallas_call(
        gate_up_kernel,
        grid=(token_count // tile,),
        in_specs=[
            pl.BlockSpec((tile, 2), lambda i: (i, 0)),
            pl.BlockSpec((tile, width), lambda i: (i, 0)),
            weight_spec,
            weight_spec,
        ],
        out_specs=[out_spec, out_spec],
        out_shape=[out, out],
    )(route_ids, gathered, gate_weight, up_weight)


def down(route_ids, hidden_all, down_weight, tile):
    _, token_count, hidden_width = hidden_all.shape
    experts, _, width = down_weight.shape
    return pl.pallas_call(
        down_kernel,
        grid=(token_count // tile,),
        in_specs=[
            pl.BlockSpec((tile, 2), lambda i: (i, 0)),
            pl.BlockSpec((2, tile, hidden_width), lambda i: (0, i, 0)),
            pl.BlockSpec((experts, hidden_width, width), lambda i: (0, 0, 0)),
        ],
        out_specs=pl.BlockSpec((tile, width), lambda i: (i, 0)),
        out_shape=jax.ShapeDtypeStruct((token_count, width), jnp.bfloat16),
    )(route_ids, hidden_all, down_weight)


def shards(
    tokens,
    gate_weight,
    up_weight,
    down_weight,
    route_ids,
    route_weight,
    prefill_cache,
    dest_col,
    dest_slot,
    pages_used,
):
    decode_cache = move_pages(prefill_cache, dest_col, dest_slot, pages_used)
    gathered = lax.all_gather(tokens, "row", axis=0, tiled=True)
    token_count = gathered.shape[0]
    hidden_width = gate_weight.shape[2]
    gate_part, up_part = gate_up(route_ids, gathered, gate_weight, up_weight, 256)
    gate_sum = lax.psum_scatter(
        gate_part.reshape(2 * token_count, hidden_width), "col", scatter_dimension=0, tiled=True
    ).astype(jnp.float32)
    up_sum = lax.psum_scatter(
        up_part.reshape(2 * token_count, hidden_width), "col", scatter_dimension=0, tiled=True
    ).astype(jnp.float32)
    share_rows = gate_sum.shape[0]
    own_weight = lax.dynamic_slice_in_dim(
        route_weight.T.reshape(-1), lax.axis_index("col") * share_rows, share_rows, 0
    )
    hidden = (own_weight[:, None] * jax.nn.silu(gate_sum) * up_sum).astype(jnp.bfloat16)
    hidden_all = lax.all_gather(hidden, "col", axis=0, tiled=True).reshape(
        2, token_count, hidden_width
    )
    per_token = down(route_ids, hidden_all, down_weight, 256)
    mixed = lax.psum_scatter(per_token, "row", scatter_dimension=0, tiled=True)
    return (mixed, decode_cache)


def solution(mesh):
    in_specs = (
        P("row", "col"),
        P(None, "col", "row"),
        P(None, "col", "row"),
        P(None, "row", "col"),
        P(),
        P(),
        P(None, ("row", "col"), None, None),
        P("row", None, None),
        P("row", None, None),
        P("row", None),
    )
    out_specs = (P("row", "col"), P(None, ("row", "col"), None, None))
    return jax.shard_map(shards, mesh=mesh, in_specs=in_specs, out_specs=out_specs, check_vma=False)
```

```python
import jax
import jax.numpy as jnp
from jax import lax
from jax.sharding import PartitionSpec as P
from jax.experimental import pallas as pl


def move_pages(prefill_cache, dest_col, dest_slot, pages_used):
    col_devices = lax.axis_size("col")
    own_index = lax.axis_index("col")
    slot_count = prefill_cache.shape[1]
    per_peer = slot_count // col_devices
    dest_table = dest_col[0]
    targets = dest_slot[0]
    page_index = jnp.arange(slot_count, dtype=jnp.int32)
    same_dest = dest_table[:, :, None] == dest_table[:, None, :]
    earlier = page_index[None, :] < page_index[:, None]
    dest_rank = jnp.sum((same_dest & earlier[None]).astype(jnp.int32), axis=2)
    send_order = lax.dynamic_index_in_dim(
        dest_table * per_peer + dest_rank, own_index, 0, keepdims=False
    )
    inverse = jnp.zeros((slot_count,), jnp.int32).at[send_order].set(page_index)
    own_used = lax.dynamic_index_in_dim(pages_used[0], own_index, 0, keepdims=False)
    is_live = page_index < own_used
    masked_pages = jnp.where(
        is_live[None, :, None, None], prefill_cache, jnp.zeros((), prefill_cache.dtype)
    )
    received = lax.all_to_all(
        masked_pages[:, inverse], "col", split_axis=1, concat_axis=1, tiled=True
    )
    senders = jnp.arange(col_devices, dtype=jnp.int32)[:, None]
    arrival = jnp.where(dest_table == own_index, senders * per_peer + dest_rank, slot_count)
    slot_of_arrival = (
        jnp.zeros((slot_count + 1,), jnp.int32)
        .at[arrival.reshape(-1)]
        .set(targets.reshape(-1))[:slot_count]
    )
    source_of_slot = jnp.zeros((slot_count,), jnp.int32).at[slot_of_arrival].set(page_index)
    return received[:, source_of_slot]


def gate_up_kernel(ids_ref, x_ref, w_ref, o_ref):
    x = x_ref[...]
    ids = ids_ref[...]
    zero = jnp.zeros_like(x)
    rows = x.shape[0]
    acc = jnp.zeros((2 * rows, w_ref.shape[2]), jnp.float32)
    for e in range(w_ref.shape[0]):
        lhs = jnp.concatenate(
            [jnp.where(ids[:, 0:1] == e, x, zero), jnp.where(ids[:, 1:2] == e, x, zero)], axis=0
        )
        acc = acc + jnp.dot(lhs, w_ref[e], preferred_element_type=jnp.float32)
    o_ref[...] = acc.astype(o_ref.dtype).reshape(o_ref.shape)


def down_kernel(ids_ref, h_ref, d_ref, o_ref):
    ids = ids_ref[...]
    first = h_ref[0]
    second = h_ref[1]
    zero = jnp.zeros_like(first)
    acc = jnp.zeros(o_ref.shape, jnp.float32)
    for e in range(d_ref.shape[0]):
        lhs = jnp.where(ids[:, 0:1] == e, first, jnp.where(ids[:, 1:2] == e, second, zero))
        acc = acc + jnp.dot(lhs, d_ref[e], preferred_element_type=jnp.float32)
    o_ref[...] = acc.astype(o_ref.dtype)


def gate_up(route_ids, gathered, paired, tile):
    token_count, width = gathered.shape
    experts, _, paired_width = paired.shape
    return pl.pallas_call(
        gate_up_kernel,
        grid=(token_count // tile,),
        in_specs=[
            pl.BlockSpec((tile, 2), lambda i: (i, 0)),
            pl.BlockSpec((tile, width), lambda i: (i, 0)),
            pl.BlockSpec((experts, width, paired_width), lambda i: (0, 0, 0)),
        ],
        out_specs=pl.BlockSpec((2, tile, paired_width), lambda i: (0, i, 0)),
        out_shape=jax.ShapeDtypeStruct((2, token_count, paired_width), jnp.bfloat16),
    )(route_ids, gathered, paired)


def gather_rows(x, axis_name):
    count = lax.axis_size(axis_name)
    copies = jnp.broadcast_to(x[None], (count,) + x.shape)
    received = lax.all_to_all(copies, axis_name, 0, 0, tiled=False)
    return received.reshape((count * x.shape[0],) + x.shape[1:])


def sum_scatter_rows(x, axis_name):
    count = lax.axis_size(axis_name)
    pieces = x.reshape((count, x.shape[0] // count) + x.shape[1:])
    received = lax.all_to_all(pieces, axis_name, 0, 0, tiled=False)
    return jnp.sum(received.astype(jnp.float32), axis=0)


def down(route_ids, hidden_all, down_weight, tile):
    _, token_count, hidden_width = hidden_all.shape
    experts, _, width = down_weight.shape
    return pl.pallas_call(
        down_kernel,
        grid=(token_count // tile,),
        in_specs=[
            pl.BlockSpec((tile, 2), lambda i: (i, 0)),
            pl.BlockSpec((2, tile, hidden_width), lambda i: (0, i, 0)),
            pl.BlockSpec((experts, hidden_width, width), lambda i: (0, 0, 0)),
        ],
        out_specs=pl.BlockSpec((tile, width), lambda i: (i, 0)),
        out_shape=jax.ShapeDtypeStruct((token_count, width), jnp.bfloat16),
    )(route_ids, hidden_all, down_weight)


def shards(
    tokens,
    gate_weight,
    up_weight,
    down_weight,
    route_ids,
    route_weight,
    prefill_cache,
    dest_col,
    dest_slot,
    pages_used,
):
    decode_cache = move_pages(prefill_cache, dest_col, dest_slot, pages_used)
    gathered = gather_rows(tokens, "row")
    token_count = gathered.shape[0]
    hidden_width = gate_weight.shape[2]
    paired = jnp.concatenate([gate_weight, up_weight], axis=2)
    partial_sums = gate_up(route_ids, gathered, paired, 256)
    summed = sum_scatter_rows(partial_sums.reshape(2 * token_count, 2 * hidden_width), "col")
    share_rows = summed.shape[0]
    own_weight = lax.dynamic_slice_in_dim(
        route_weight.T.reshape(-1), lax.axis_index("col") * share_rows, share_rows, 0
    )
    hidden = (
        own_weight[:, None] * jax.nn.silu(summed[:, :hidden_width]) * summed[:, hidden_width:]
    ).astype(jnp.bfloat16)
    hidden_all = lax.all_gather(hidden, "col", axis=0, tiled=True).reshape(
        2, token_count, hidden_width
    )
    per_token = down(route_ids, hidden_all, down_weight, 256)
    mixed = sum_scatter_rows(per_token, "row").astype(jnp.bfloat16)
    return (mixed, decode_cache)


def solution(mesh):
    in_specs = (
        P("row", "col"),
        P(None, "col", "row"),
        P(None, "col", "row"),
        P(None, "row", "col"),
        P(),
        P(),
        P(None, ("row", "col"), None, None),
        P("row", None, None),
        P("row", None, None),
        P("row", None),
    )
    out_specs = (P("row", "col"), P(None, ("row", "col"), None, None))
    return jax.shard_map(shards, mesh=mesh, in_specs=in_specs, out_specs=out_specs, check_vma=False)
```

```python
import jax
import jax.numpy as jnp
from jax import lax
from jax.sharding import PartitionSpec as P
from jax.experimental import pallas as pl
from jax.experimental.pallas import tpu as pltpu


def move_pages(prefill_cache, dest_col, dest_slot, pages_used):
    col_devices = lax.axis_size("col")
    own_index = lax.axis_index("col")
    slot_count = prefill_cache.shape[1]
    per_peer = slot_count // col_devices
    dest_table = dest_col[0]
    targets = dest_slot[0]
    page_index = jnp.arange(slot_count, dtype=jnp.int32)
    same_dest = dest_table[:, :, None] == dest_table[:, None, :]
    earlier = page_index[None, :] < page_index[:, None]
    dest_rank = jnp.sum((same_dest & earlier[None]).astype(jnp.int32), axis=2)
    send_order = lax.dynamic_index_in_dim(
        dest_table * per_peer + dest_rank, own_index, 0, keepdims=False
    )
    inverse = jnp.zeros((slot_count,), jnp.int32).at[send_order].set(page_index)
    own_used = lax.dynamic_index_in_dim(pages_used[0], own_index, 0, keepdims=False)
    is_live = page_index < own_used
    masked_pages = jnp.where(
        is_live[None, :, None, None], prefill_cache, jnp.zeros((), prefill_cache.dtype)
    )
    received = lax.all_to_all(
        masked_pages[:, inverse], "col", split_axis=1, concat_axis=1, tiled=True
    )
    senders = jnp.arange(col_devices, dtype=jnp.int32)[:, None]
    arrival = jnp.where(dest_table == own_index, senders * per_peer + dest_rank, slot_count)
    slot_of_arrival = (
        jnp.zeros((slot_count + 1,), jnp.int32)
        .at[arrival.reshape(-1)]
        .set(targets.reshape(-1))[:slot_count]
    )
    source_of_slot = jnp.zeros((slot_count,), jnp.int32).at[slot_of_arrival].set(page_index)
    return received[:, source_of_slot]


def gate_up_kernel(ids_ref, x_ref, w_ref, o_ref):
    x = x_ref[...]
    ids = ids_ref[...]
    zero = jnp.zeros_like(x)
    rows = x.shape[0]
    acc = jnp.zeros((2 * rows, w_ref.shape[2]), jnp.float32)
    for e in range(w_ref.shape[0]):
        lhs = jnp.concatenate(
            [jnp.where(ids[:, 0:1] == e, x, zero), jnp.where(ids[:, 1:2] == e, x, zero)], axis=0
        )
        acc = acc + jnp.dot(lhs, w_ref[e], preferred_element_type=jnp.float32)
    o_ref[...] = acc.astype(o_ref.dtype).reshape(o_ref.shape)


def hidden_kernel(w_ref, s_ref, o_ref, h_scr):
    @pl.when(pl.program_id(1) == 0)
    def _():
        summed = jnp.sum(s_ref[...].astype(jnp.float32), axis=0)
        half = summed.shape[1] // 2
        gate = summed[:, :half]
        hidden = w_ref[...] * (gate / (1.0 + jnp.exp(-gate))) * summed[:, half:]
        h_scr[...] = hidden.astype(h_scr.dtype)

    o_ref[0] = h_scr[...]


def down_kernel(ids_ref, h_ref, d_ref, o_ref):
    ids = ids_ref[...]
    first = h_ref[0]
    second = h_ref[1]
    zero = jnp.zeros_like(first)
    acc = jnp.zeros(o_ref.shape, jnp.float32)
    for e in range(d_ref.shape[0]):
        lhs = jnp.where(ids[:, 0:1] == e, first, jnp.where(ids[:, 1:2] == e, second, zero))
        acc = acc + jnp.dot(lhs, d_ref[e], preferred_element_type=jnp.float32)
    o_ref[...] = acc.astype(o_ref.dtype)


def gate_up(route_ids, gathered, paired, tile):
    token_count, width = gathered.shape
    experts, _, paired_width = paired.shape
    return pl.pallas_call(
        gate_up_kernel,
        grid=(token_count // tile,),
        in_specs=[
            pl.BlockSpec((tile, 2), lambda i: (i, 0)),
            pl.BlockSpec((tile, width), lambda i: (i, 0)),
            pl.BlockSpec((experts, width, paired_width), lambda i: (0, 0, 0)),
        ],
        out_specs=pl.BlockSpec((2, tile, paired_width), lambda i: (0, i, 0)),
        out_shape=jax.ShapeDtypeStruct((2, token_count, paired_width), jnp.bfloat16),
    )(route_ids, gathered, paired)


def gather_rows(x, axis_name):
    count = lax.axis_size(axis_name)
    copies = jnp.broadcast_to(x[None], (count,) + x.shape)
    received = lax.all_to_all(copies, axis_name, 0, 0, tiled=False)
    return received.reshape((count * x.shape[0],) + x.shape[1:])


def sum_scatter_rows(x, axis_name):
    count = lax.axis_size(axis_name)
    pieces = x.reshape((count, x.shape[0] // count) + x.shape[1:])
    received = lax.all_to_all(pieces, axis_name, 0, 0, tiled=False)
    return jnp.sum(received.astype(jnp.float32), axis=0)


def hidden_copies(own_weight, received, hidden_width, block):
    count, share_rows, paired_width = received.shape
    return pl.pallas_call(
        hidden_kernel,
        grid=(share_rows // block, count),
        in_specs=[
            pl.BlockSpec((block, 1), lambda i, j: (i, 0)),
            pl.BlockSpec((count, block, paired_width), lambda i, j: (0, i, 0)),
        ],
        out_specs=pl.BlockSpec((1, block, hidden_width), lambda i, j: (j, i, 0)),
        out_shape=jax.ShapeDtypeStruct((count, share_rows, hidden_width), jnp.bfloat16),
        scratch_shapes=[pltpu.VMEM((block, hidden_width), jnp.bfloat16)],
    )(own_weight, received)


def down(route_ids, hidden_all, down_weight, tile):
    _, token_count, hidden_width = hidden_all.shape
    experts, _, width = down_weight.shape
    return pl.pallas_call(
        down_kernel,
        grid=(token_count // tile,),
        in_specs=[
            pl.BlockSpec((tile, 2), lambda i: (i, 0)),
            pl.BlockSpec((2, tile, hidden_width), lambda i: (0, i, 0)),
            pl.BlockSpec((experts, hidden_width, width), lambda i: (0, 0, 0)),
        ],
        out_specs=pl.BlockSpec((tile, width), lambda i: (i, 0)),
        out_shape=jax.ShapeDtypeStruct((token_count, width), jnp.bfloat16),
    )(route_ids, hidden_all, down_weight)


def shards(
    tokens,
    gate_weight,
    up_weight,
    down_weight,
    route_ids,
    route_weight,
    prefill_cache,
    dest_col,
    dest_slot,
    pages_used,
):
    decode_cache = move_pages(prefill_cache, dest_col, dest_slot, pages_used)
    gathered = gather_rows(tokens, "row")
    token_count = gathered.shape[0]
    hidden_width = gate_weight.shape[2]
    experts, width, _ = gate_weight.shape
    padded_width = -(-hidden_width // 128) * 128
    pad = jnp.zeros((experts, width, padded_width - hidden_width), gate_weight.dtype)
    paired = jnp.concatenate([gate_weight, pad, up_weight, pad], axis=2)
    partial_sums = gate_up(route_ids, gathered, paired, 256)
    col_count = lax.axis_size("col")
    share_rows = 2 * token_count // col_count
    received = lax.all_to_all(
        partial_sums.reshape(col_count, share_rows, 2 * padded_width), "col", 0, 0, tiled=False
    )
    own_weight = lax.dynamic_slice_in_dim(
        route_weight.T.reshape(-1), lax.axis_index("col") * share_rows, share_rows, 0
    ).reshape(share_rows, 1)
    copies = hidden_copies(own_weight, received, padded_width, 64)
    hidden_all = lax.all_to_all(copies, "col", 0, 0, tiled=False).reshape(
        2, token_count, padded_width
    )
    down_pad = jnp.zeros(
        (experts, padded_width - hidden_width, down_weight.shape[2]), down_weight.dtype
    )
    down_weight = jnp.concatenate([down_weight, down_pad], axis=1)
    per_token = down(route_ids, hidden_all, down_weight, 256)
    mixed = sum_scatter_rows(per_token, "row").astype(jnp.bfloat16)
    return (mixed, decode_cache)


def solution(mesh):
    in_specs = (
        P("row", "col"),
        P(None, "col", "row"),
        P(None, "col", "row"),
        P(None, "row", "col"),
        P(),
        P(),
        P(None, ("row", "col"), None, None),
        P("row", None, None),
        P("row", None, None),
        P("row", None),
    )
    out_specs = (P("row", "col"), P(None, ("row", "col"), None, None))
    return jax.shard_map(shards, mesh=mesh, in_specs=in_specs, out_specs=out_specs, check_vma=False)
```

```python
import jax
import jax.numpy as jnp
from jax import lax
from jax.sharding import PartitionSpec as P
from jax.experimental import pallas as pl


def move_pages(prefill_cache, dest_col, dest_slot, pages_used):
    col_devices = lax.axis_size("col")
    own_index = lax.axis_index("col")
    slot_count = prefill_cache.shape[1]
    per_peer = slot_count // col_devices
    dest_table = dest_col[0]
    targets = dest_slot[0]
    page_index = jnp.arange(slot_count, dtype=jnp.int32)
    same_dest = dest_table[:, :, None] == dest_table[:, None, :]
    earlier = page_index[None, :] < page_index[:, None]
    dest_rank = jnp.sum((same_dest & earlier[None]).astype(jnp.int32), axis=2)
    send_order = lax.dynamic_index_in_dim(
        dest_table * per_peer + dest_rank, own_index, 0, keepdims=False
    )
    inverse = jnp.zeros((slot_count,), jnp.int32).at[send_order].set(page_index)
    own_used = lax.dynamic_index_in_dim(pages_used[0], own_index, 0, keepdims=False)
    is_live = page_index < own_used
    masked_pages = jnp.where(
        is_live[None, :, None, None], prefill_cache, jnp.zeros((), prefill_cache.dtype)
    )
    received = lax.all_to_all(
        masked_pages[:, inverse], "col", split_axis=1, concat_axis=1, tiled=True
    )
    senders = jnp.arange(col_devices, dtype=jnp.int32)[:, None]
    arrival = jnp.where(dest_table == own_index, senders * per_peer + dest_rank, slot_count)
    slot_of_arrival = (
        jnp.zeros((slot_count + 1,), jnp.int32)
        .at[arrival.reshape(-1)]
        .set(targets.reshape(-1))[:slot_count]
    )
    source_of_slot = jnp.zeros((slot_count,), jnp.int32).at[slot_of_arrival].set(page_index)
    return received[:, source_of_slot]


def gate_up_kernel(ids_ref, x_ref, w_ref, o_ref):
    x = x_ref[...]
    ids = ids_ref[...]
    zero = jnp.zeros_like(x)
    rows = x.shape[0]
    acc = jnp.zeros((2 * rows, w_ref.shape[2]), jnp.float32)
    for e in range(w_ref.shape[0]):
        lhs = jnp.concatenate(
            [jnp.where(ids[:, 0:1] == e, x, zero), jnp.where(ids[:, 1:2] == e, x, zero)], axis=0
        )
        acc = acc + jnp.dot(lhs, w_ref[e], preferred_element_type=jnp.float32)
    o_ref[...] = acc.astype(o_ref.dtype).reshape(o_ref.shape)


def down_kernel(ids_ref, h_ref, d_ref, o_ref):
    ids = ids_ref[...]
    first = h_ref[0]
    second = h_ref[1]
    zero = jnp.zeros_like(first)
    acc = jnp.zeros(o_ref.shape, jnp.float32)
    for e in range(d_ref.shape[0]):
        lhs = jnp.where(ids[:, 0:1] == e, first, jnp.where(ids[:, 1:2] == e, second, zero))
        acc = acc + jnp.dot(lhs, d_ref[e], preferred_element_type=jnp.float32)
    o_ref[...] = acc.astype(o_ref.dtype)


def gate_up(route_ids, gathered, paired, tile):
    token_count, width = gathered.shape
    experts, _, paired_width = paired.shape
    return pl.pallas_call(
        gate_up_kernel,
        grid=(token_count // tile,),
        in_specs=[
            pl.BlockSpec((tile, 2), lambda i: (i, 0)),
            pl.BlockSpec((tile, width), lambda i: (i, 0)),
            pl.BlockSpec((experts, width, paired_width), lambda i: (0, 0, 0)),
        ],
        out_specs=pl.BlockSpec((2, tile, paired_width), lambda i: (0, i, 0)),
        out_shape=jax.ShapeDtypeStruct((2, token_count, paired_width), jnp.bfloat16),
    )(route_ids, gathered, paired)


def gather_rows(x, axis_name):
    count = lax.axis_size(axis_name)
    copies = jnp.broadcast_to(x[None], (count,) + x.shape)
    received = lax.all_to_all(copies, axis_name, 0, 0, tiled=False)
    return received.reshape((count * x.shape[0],) + x.shape[1:])


def sum_scatter_rows(x, axis_name):
    count = lax.axis_size(axis_name)
    pieces = x.reshape((count, x.shape[0] // count) + x.shape[1:])
    received = lax.all_to_all(pieces, axis_name, 0, 0, tiled=False)
    return jnp.sum(received.astype(jnp.float32), axis=0)


def down(route_ids, hidden_all, down_weight, tile):
    _, token_count, hidden_width = hidden_all.shape
    experts, _, width = down_weight.shape
    return pl.pallas_call(
        down_kernel,
        grid=(token_count // tile,),
        in_specs=[
            pl.BlockSpec((tile, 2), lambda i: (i, 0)),
            pl.BlockSpec((2, tile, hidden_width), lambda i: (0, i, 0)),
            pl.BlockSpec((experts, hidden_width, width), lambda i: (0, 0, 0)),
        ],
        out_specs=pl.BlockSpec((tile, width), lambda i: (i, 0)),
        out_shape=jax.ShapeDtypeStruct((token_count, width), jnp.bfloat16),
    )(route_ids, hidden_all, down_weight)


def shards(
    tokens,
    gate_weight,
    up_weight,
    down_weight,
    route_ids,
    route_weight,
    prefill_cache,
    dest_col,
    dest_slot,
    pages_used,
):
    decode_cache = move_pages(prefill_cache, dest_col, dest_slot, pages_used)
    gathered = gather_rows(tokens, "row")
    token_count = gathered.shape[0]
    hidden_width = gate_weight.shape[2]
    paired = jnp.concatenate([gate_weight, up_weight], axis=2)
    partial_sums = gate_up(route_ids, gathered, paired, 256)
    summed = lax.psum_scatter(
        partial_sums.reshape(2 * token_count, 2 * hidden_width), "col", scatter_dimension=0, tiled=True
    ).astype(jnp.float32)
    share_rows = summed.shape[0]
    own_weight = lax.dynamic_slice_in_dim(
        route_weight.T.reshape(-1), lax.axis_index("col") * share_rows, share_rows, 0
    )
    hidden = (
        own_weight[:, None] * jax.nn.silu(summed[:, :hidden_width]) * summed[:, hidden_width:]
    ).astype(jnp.bfloat16)
    hidden_all = lax.all_gather(hidden, "col", axis=0, tiled=True).reshape(
        2, token_count, hidden_width
    )
    per_token = down(route_ids, hidden_all, down_weight, 256)
    mixed = sum_scatter_rows(per_token, "row").astype(jnp.bfloat16)
    return (mixed, decode_cache)


def solution(mesh):
    in_specs = (
        P("row", "col"),
        P(None, "col", "row"),
        P(None, "col", "row"),
        P(None, "row", "col"),
        P(),
        P(),
        P(None, ("row", "col"), None, None),
        P("row", None, None),
        P("row", None, None),
        P("row", None),
    )
    out_specs = (P("row", "col"), P(None, ("row", "col"), None, None))
    return jax.shard_map(shards, mesh=mesh, in_specs=in_specs, out_specs=out_specs, check_vma=False)
```

```python
import jax
import jax.numpy as jnp
from jax import lax
from jax.sharding import PartitionSpec as P
from jax.experimental import pallas as pl


def move_pages(prefill_cache, dest_col, dest_slot, pages_used):
    col_devices = lax.axis_size("col")
    own_index = lax.axis_index("col")
    slot_count = prefill_cache.shape[1]
    per_peer = slot_count // col_devices
    dest_table = dest_col[0]
    targets = dest_slot[0]
    page_index = jnp.arange(slot_count, dtype=jnp.int32)
    same_dest = dest_table[:, :, None] == dest_table[:, None, :]
    earlier = page_index[None, :] < page_index[:, None]
    dest_rank = jnp.sum((same_dest & earlier[None]).astype(jnp.int32), axis=2)
    send_order = lax.dynamic_index_in_dim(
        dest_table * per_peer + dest_rank, own_index, 0, keepdims=False
    )
    inverse = jnp.zeros((slot_count,), jnp.int32).at[send_order].set(page_index)
    own_used = lax.dynamic_index_in_dim(pages_used[0], own_index, 0, keepdims=False)
    is_live = page_index < own_used
    masked_pages = jnp.where(
        is_live[None, :, None, None], prefill_cache, jnp.zeros((), prefill_cache.dtype)
    )
    received = lax.all_to_all(
        masked_pages[:, inverse], "col", split_axis=1, concat_axis=1, tiled=True
    )
    senders = jnp.arange(col_devices, dtype=jnp.int32)[:, None]
    arrival = jnp.where(dest_table == own_index, senders * per_peer + dest_rank, slot_count)
    slot_of_arrival = (
        jnp.zeros((slot_count + 1,), jnp.int32)
        .at[arrival.reshape(-1)]
        .set(targets.reshape(-1))[:slot_count]
    )
    source_of_slot = jnp.zeros((slot_count,), jnp.int32).at[slot_of_arrival].set(page_index)
    return received[:, source_of_slot]


def gate_up_kernel(ids_ref, x_ref, w_ref, o_ref):
    x = x_ref[...]
    ids = ids_ref[...]
    zero = jnp.zeros_like(x)
    rows = x.shape[0]
    acc = jnp.zeros((2 * rows, w_ref.shape[2]), jnp.float32)
    for e in range(w_ref.shape[0]):
        lhs = jnp.concatenate(
            [jnp.where(ids[:, 0:1] == e, x, zero), jnp.where(ids[:, 1:2] == e, x, zero)], axis=0
        )
        acc = acc + jnp.dot(lhs, w_ref[e], preferred_element_type=jnp.float32)
    o_ref[...] = acc.astype(o_ref.dtype).reshape(o_ref.shape)


def down_kernel(ids_ref, h_ref, d_ref, o_ref):
    ids = ids_ref[...]
    first = h_ref[0]
    second = h_ref[1]
    zero = jnp.zeros_like(first)
    acc = jnp.zeros(o_ref.shape, jnp.float32)
    for e in range(d_ref.shape[0]):
        lhs = jnp.where(ids[:, 0:1] == e, first, jnp.where(ids[:, 1:2] == e, second, zero))
        acc = acc + jnp.dot(lhs, d_ref[e], preferred_element_type=jnp.float32)
    o_ref[...] = acc.astype(o_ref.dtype)


def gate_up(route_ids, gathered, paired, tile):
    token_count, width = gathered.shape
    experts, _, paired_width = paired.shape
    return pl.pallas_call(
        gate_up_kernel,
        grid=(token_count // tile,),
        in_specs=[
            pl.BlockSpec((tile, 2), lambda i: (i, 0)),
            pl.BlockSpec((tile, width), lambda i: (i, 0)),
            pl.BlockSpec((experts, width, paired_width), lambda i: (0, 0, 0)),
        ],
        out_specs=pl.BlockSpec((2, tile, paired_width), lambda i: (0, i, 0)),
        out_shape=jax.ShapeDtypeStruct((2, token_count, paired_width), jnp.bfloat16),
    )(route_ids, gathered, paired)


def gather_rows(x, axis_name):
    count = lax.axis_size(axis_name)
    copies = jnp.broadcast_to(x[None], (count,) + x.shape)
    received = lax.all_to_all(copies, axis_name, 0, 0, tiled=False)
    return received.reshape((count * x.shape[0],) + x.shape[1:])


def sum_scatter_rows(x, axis_name):
    count = lax.axis_size(axis_name)
    pieces = x.reshape((count, x.shape[0] // count) + x.shape[1:])
    received = lax.all_to_all(pieces, axis_name, 0, 0, tiled=False)
    return jnp.sum(received.astype(jnp.float32), axis=0)


def down(route_ids, hidden_all, down_weight, tile):
    _, token_count, hidden_width = hidden_all.shape
    experts, _, width = down_weight.shape
    return pl.pallas_call(
        down_kernel,
        grid=(token_count // tile,),
        in_specs=[
            pl.BlockSpec((tile, 2), lambda i: (i, 0)),
            pl.BlockSpec((2, tile, hidden_width), lambda i: (0, i, 0)),
            pl.BlockSpec((experts, hidden_width, width), lambda i: (0, 0, 0)),
        ],
        out_specs=pl.BlockSpec((tile, width), lambda i: (i, 0)),
        out_shape=jax.ShapeDtypeStruct((token_count, width), jnp.bfloat16),
    )(route_ids, hidden_all, down_weight)


def shards(
    tokens,
    gate_weight,
    up_weight,
    down_weight,
    route_ids,
    route_weight,
    prefill_cache,
    dest_col,
    dest_slot,
    pages_used,
):
    decode_cache = move_pages(prefill_cache, dest_col, dest_slot, pages_used)
    gathered = gather_rows(tokens, "row")
    token_count = gathered.shape[0]
    hidden_width = gate_weight.shape[2]
    paired = jnp.concatenate([gate_weight, up_weight], axis=2)
    col_count = lax.axis_size("col")
    share = 2 * token_count // col_count
    lead = share * 5 // 8
    blocks = token_count // share
    tokens_by_block = gathered.reshape(blocks, share, gathered.shape[1])
    ids_by_block = route_ids.reshape(blocks, share, 2)
    lead_part = gate_up(
        ids_by_block[:, :lead].reshape(-1, 2),
        tokens_by_block[:, :lead].reshape(-1, gathered.shape[1]),
        paired,
        lead,
    )
    lead_sum = lax.psum_scatter(
        lead_part.reshape(col_count * lead, 2 * hidden_width), "col", scatter_dimension=0, tiled=True
    ).astype(jnp.float32)
    tail_part = gate_up(
        ids_by_block[:, lead:].reshape(-1, 2),
        tokens_by_block[:, lead:].reshape(-1, gathered.shape[1]),
        paired,
        share - lead,
    )
    tail_sum = sum_scatter_rows(tail_part.reshape(col_count * (share - lead), 2 * hidden_width), "col")
    summed = jnp.concatenate([lead_sum, tail_sum], axis=0)
    share_rows = summed.shape[0]
    own_weight = lax.dynamic_slice_in_dim(
        route_weight.T.reshape(-1), lax.axis_index("col") * share_rows, share_rows, 0
    )
    hidden = (
        own_weight[:, None] * jax.nn.silu(summed[:, :hidden_width]) * summed[:, hidden_width:]
    ).astype(jnp.bfloat16)
    hidden_all = lax.all_gather(hidden, "col", axis=0, tiled=True).reshape(
        2, token_count, hidden_width
    )
    per_token = down(route_ids, hidden_all, down_weight, 256)
    mixed = sum_scatter_rows(per_token, "row").astype(jnp.bfloat16)
    return (mixed, decode_cache)


def solution(mesh):
    in_specs = (
        P("row", "col"),
        P(None, "col", "row"),
        P(None, "col", "row"),
        P(None, "row", "col"),
        P(),
        P(),
        P(None, ("row", "col"), None, None),
        P("row", None, None),
        P("row", None, None),
        P("row", None),
    )
    out_specs = (P("row", "col"), P(None, ("row", "col"), None, None))
    return jax.shard_map(shards, mesh=mesh, in_specs=in_specs, out_specs=out_specs, check_vma=False)
```

```python
import jax
import jax.numpy as jnp
from jax import lax
from jax.sharding import PartitionSpec as P
from jax.experimental import pallas as pl


def move_pages(prefill_cache, dest_col, dest_slot, pages_used):
    col_devices = lax.axis_size("col")
    own_index = lax.axis_index("col")
    slot_count = prefill_cache.shape[1]
    per_peer = slot_count // col_devices
    dest_table = dest_col[0]
    targets = dest_slot[0]
    page_index = jnp.arange(slot_count, dtype=jnp.int32)
    same_dest = dest_table[:, :, None] == dest_table[:, None, :]
    earlier = page_index[None, :] < page_index[:, None]
    dest_rank = jnp.sum((same_dest & earlier[None]).astype(jnp.int32), axis=2)
    send_order = lax.dynamic_index_in_dim(
        dest_table * per_peer + dest_rank, own_index, 0, keepdims=False
    )
    inverse = jnp.zeros((slot_count,), jnp.int32).at[send_order].set(page_index)
    own_used = lax.dynamic_index_in_dim(pages_used[0], own_index, 0, keepdims=False)
    is_live = page_index < own_used
    masked_pages = jnp.where(
        is_live[None, :, None, None], prefill_cache, jnp.zeros((), prefill_cache.dtype)
    )
    received = lax.all_to_all(
        masked_pages[:, inverse], "col", split_axis=1, concat_axis=1, tiled=True
    )
    senders = jnp.arange(col_devices, dtype=jnp.int32)[:, None]
    arrival = jnp.where(dest_table == own_index, senders * per_peer + dest_rank, slot_count)
    slot_of_arrival = (
        jnp.zeros((slot_count + 1,), jnp.int32)
        .at[arrival.reshape(-1)]
        .set(targets.reshape(-1))[:slot_count]
    )
    source_of_slot = jnp.zeros((slot_count,), jnp.int32).at[slot_of_arrival].set(page_index)
    return received[:, source_of_slot]


def gate_up_kernel(ids_ref, x_ref, w_ref, o_ref):
    x = x_ref[...]
    ids = ids_ref[...]
    zero = jnp.zeros_like(x)
    rows = x.shape[0]
    acc = jnp.zeros((2 * rows, w_ref.shape[2]), jnp.float32)
    for e in range(w_ref.shape[0]):
        lhs = jnp.concatenate(
            [jnp.where(ids[:, 0:1] == e, x, zero), jnp.where(ids[:, 1:2] == e, x, zero)], axis=0
        )
        acc = acc + jnp.dot(lhs, w_ref[e], preferred_element_type=jnp.float32)
    o_ref[...] = acc.astype(o_ref.dtype).reshape(o_ref.shape)


def down_kernel(ids_ref, h_ref, d_ref, o_ref):
    ids = ids_ref[...]
    first = h_ref[0]
    second = h_ref[1]
    zero = jnp.zeros_like(first)
    acc = jnp.zeros(o_ref.shape, jnp.float32)
    for e in range(d_ref.shape[0]):
        lhs = jnp.where(ids[:, 0:1] == e, first, jnp.where(ids[:, 1:2] == e, second, zero))
        acc = acc + jnp.dot(lhs, d_ref[e], preferred_element_type=jnp.float32)
    o_ref[...] = acc.astype(o_ref.dtype)


def gate_up(route_ids, gathered, paired, tile):
    token_count, width = gathered.shape
    experts, _, paired_width = paired.shape
    return pl.pallas_call(
        gate_up_kernel,
        grid=(token_count // tile,),
        in_specs=[
            pl.BlockSpec((tile, 2), lambda i: (i, 0)),
            pl.BlockSpec((tile, width), lambda i: (i, 0)),
            pl.BlockSpec((experts, width, paired_width), lambda i: (0, 0, 0)),
        ],
        out_specs=pl.BlockSpec((2, tile, paired_width), lambda i: (0, i, 0)),
        out_shape=jax.ShapeDtypeStruct((2, token_count, paired_width), jnp.bfloat16),
    )(route_ids, gathered, paired)


def gather_rows(x, axis_name):
    count = lax.axis_size(axis_name)
    copies = jnp.broadcast_to(x[None], (count,) + x.shape)
    received = lax.all_to_all(copies, axis_name, 0, 0, tiled=False)
    return received.reshape((count * x.shape[0],) + x.shape[1:])


def sum_scatter_rows(x, axis_name):
    count = lax.axis_size(axis_name)
    pieces = x.reshape((count, x.shape[0] // count) + x.shape[1:])
    received = lax.all_to_all(pieces, axis_name, 0, 0, tiled=False)
    return jnp.sum(received.astype(jnp.float32), axis=0)


def down(route_ids, hidden_all, down_weight, tile):
    _, token_count, hidden_width = hidden_all.shape
    experts, _, width = down_weight.shape
    return pl.pallas_call(
        down_kernel,
        grid=(token_count // tile,),
        in_specs=[
            pl.BlockSpec((tile, 2), lambda i: (i, 0)),
            pl.BlockSpec((2, tile, hidden_width), lambda i: (0, i, 0)),
            pl.BlockSpec((experts, hidden_width, width), lambda i: (0, 0, 0)),
        ],
        out_specs=pl.BlockSpec((tile, width), lambda i: (i, 0)),
        out_shape=jax.ShapeDtypeStruct((token_count, width), jnp.bfloat16),
    )(route_ids, hidden_all, down_weight)


def col_perm(axis_name, move):
    count = lax.axis_size(axis_name)
    return [(c, move(c)) for c in range(count)]


def x_step(c, step):
    return ((c // 4 + step) % 4) * 4 + c % 4


def pick(chunks, index, axis=0):
    return lax.dynamic_index_in_dim(chunks, index, axis, keepdims=False)


def ring_reduce(chunks, xi, axis_name, direction):
    count = chunks.shape[0]
    perm = col_perm(axis_name, lambda c: x_step(c, direction))
    cur = pick(chunks, (xi - direction) % count)
    for s in range(1, count):
        recv = lax.ppermute(cur, axis_name, perm)
        cur = recv.astype(jnp.float32) + pick(chunks, (xi - direction * (s + 1)) % count).astype(
            jnp.float32
        )
        if s < count - 1:
            cur = cur.astype(chunks.dtype)
    return cur


def ring_gather(block, xi, axis_name, direction, count):
    perm = col_perm(axis_name, lambda c: x_step(c, direction))
    out = jnp.zeros((count,) + block.shape, block.dtype)
    out = lax.dynamic_update_index_in_dim(out, block, xi, 0)
    cur = block
    for s in range(1, count):
        cur = lax.ppermute(cur, axis_name, perm)
        out = lax.dynamic_update_index_in_dim(out, cur, (xi - direction * s) % count, 0)
    return out


def col_reduce_scatter(partial, axis_name):
    c = lax.axis_index(axis_name)
    xi, zi, co = c // 4, (c // 2) % 2, c % 2
    rows = partial.shape[0] // 16
    blocks = partial.reshape(4, 2, 2, rows, partial.shape[1])
    recv = lax.ppermute(pick(blocks, 1 - co, 2), axis_name, col_perm(axis_name, lambda q: q ^ 1))
    core_sum = (pick(blocks, co, 2).astype(jnp.float32) + recv.astype(jnp.float32)).astype(
        partial.dtype
    )
    half = rows // 2
    plus = ring_reduce(core_sum[:, :, :half], xi, axis_name, 1)
    minus = ring_reduce(core_sum[:, :, half:], xi, axis_name, -1)
    x_sum = jnp.concatenate([plus, minus], axis=1)
    recv = lax.ppermute(
        pick(x_sum, 1 - zi).astype(partial.dtype), axis_name, col_perm(axis_name, lambda q: q ^ 2)
    )
    return pick(x_sum, zi) + recv.astype(jnp.float32)


def col_all_gather(block, axis_name):
    c = lax.axis_index(axis_name)
    xi, zi, co = c // 4, (c // 2) % 2, c % 2
    recv = lax.ppermute(block, axis_name, col_perm(axis_name, lambda q: q ^ 2))
    z_pair = jnp.where(zi == 0, jnp.stack([block, recv]), jnp.stack([recv, block]))
    half = block.shape[0] // 2
    plus = ring_gather(z_pair[:, :half], xi, axis_name, 1, 4)
    minus = ring_gather(z_pair[:, half:], xi, axis_name, -1, 4)
    x_all = jnp.concatenate([plus, minus], axis=2)
    recv = lax.ppermute(x_all, axis_name, col_perm(axis_name, lambda q: q ^ 1))
    full = jnp.where(co == 0, jnp.stack([x_all, recv], axis=2), jnp.stack([recv, x_all], axis=2))
    return full.reshape((-1,) + block.shape[1:])


def shards(
    tokens,
    gate_weight,
    up_weight,
    down_weight,
    route_ids,
    route_weight,
    prefill_cache,
    dest_col,
    dest_slot,
    pages_used,
):
    decode_cache = move_pages(prefill_cache, dest_col, dest_slot, pages_used)
    gathered = gather_rows(tokens, "row")
    token_count = gathered.shape[0]
    hidden_width = gate_weight.shape[2]
    paired = jnp.concatenate([gate_weight, up_weight], axis=2)
    partial_sums = gate_up(route_ids, gathered, paired, 256)
    summed = col_reduce_scatter(partial_sums.reshape(2 * token_count, 2 * hidden_width), "col")
    share_rows = summed.shape[0]
    own_weight = lax.dynamic_slice_in_dim(
        route_weight.T.reshape(-1), lax.axis_index("col") * share_rows, share_rows, 0
    )
    hidden = (
        own_weight[:, None] * jax.nn.silu(summed[:, :hidden_width]) * summed[:, hidden_width:]
    ).astype(jnp.bfloat16)
    hidden_all = col_all_gather(hidden, "col").reshape(
        2, token_count, hidden_width
    )
    per_token = down(route_ids, hidden_all, down_weight, 256)
    mixed = sum_scatter_rows(per_token, "row").astype(jnp.bfloat16)
    return (mixed, decode_cache)


def solution(mesh):
    in_specs = (
        P("row", "col"),
        P(None, "col", "row"),
        P(None, "col", "row"),
        P(None, "row", "col"),
        P(),
        P(),
        P(None, ("row", "col"), None, None),
        P("row", None, None),
        P("row", None, None),
        P("row", None),
    )
    out_specs = (P("row", "col"), P(None, ("row", "col"), None, None))
    return jax.shard_map(shards, mesh=mesh, in_specs=in_specs, out_specs=out_specs, check_vma=False)
```

```python
import jax
import jax.numpy as jnp
from jax import lax
from jax.sharding import PartitionSpec as P
from jax.experimental import pallas as pl
from jax.experimental.pallas import tpu as pltpu


def move_pages(prefill_cache, dest_col, dest_slot, pages_used):
    col_devices = lax.axis_size("col")
    own_index = lax.axis_index("col")
    slot_count = prefill_cache.shape[1]
    per_peer = slot_count // col_devices
    dest_table = dest_col[0]
    targets = dest_slot[0]
    page_index = jnp.arange(slot_count, dtype=jnp.int32)
    same_dest = dest_table[:, :, None] == dest_table[:, None, :]
    earlier = page_index[None, :] < page_index[:, None]
    dest_rank = jnp.sum((same_dest & earlier[None]).astype(jnp.int32), axis=2)
    send_order = lax.dynamic_index_in_dim(
        dest_table * per_peer + dest_rank, own_index, 0, keepdims=False
    )
    inverse = jnp.zeros((slot_count,), jnp.int32).at[send_order].set(page_index)
    own_used = lax.dynamic_index_in_dim(pages_used[0], own_index, 0, keepdims=False)
    is_live = page_index < own_used
    masked_pages = jnp.where(
        is_live[None, :, None, None], prefill_cache, jnp.zeros((), prefill_cache.dtype)
    )
    received = lax.all_to_all(
        masked_pages[:, inverse], "col", split_axis=1, concat_axis=1, tiled=True
    )
    senders = jnp.arange(col_devices, dtype=jnp.int32)[:, None]
    arrival = jnp.where(dest_table == own_index, senders * per_peer + dest_rank, slot_count)
    slot_of_arrival = (
        jnp.zeros((slot_count + 1,), jnp.int32)
        .at[arrival.reshape(-1)]
        .set(targets.reshape(-1))[:slot_count]
    )
    source_of_slot = jnp.zeros((slot_count,), jnp.int32).at[slot_of_arrival].set(page_index)
    return received[:, source_of_slot]


def gate_up_kernel(sel_ref, ids_ref, x_ref, w_ref, o_ref):
    x = x_ref[...]
    ids = ids_ref[...]
    zero = jnp.zeros_like(x)
    rows = x.shape[0]
    acc = jnp.zeros((2 * rows, w_ref.shape[2]), jnp.float32)
    for e in range(w_ref.shape[0]):
        lhs = jnp.concatenate(
            [jnp.where(ids[:, 0:1] == e, x, zero), jnp.where(ids[:, 1:2] == e, x, zero)], axis=0
        )
        acc = acc + jnp.dot(lhs, w_ref[e], preferred_element_type=jnp.float32)
    o_ref[...] = acc.astype(o_ref.dtype).reshape(o_ref.shape)


def down_kernel(ids_ref, h_ref, d_ref, o_ref):
    ids = ids_ref[...]
    first = h_ref[0]
    second = h_ref[1]
    zero = jnp.zeros_like(first)
    acc = jnp.zeros(o_ref.shape, jnp.float32)
    for e in range(d_ref.shape[0]):
        lhs = jnp.where(ids[:, 0:1] == e, first, jnp.where(ids[:, 1:2] == e, second, zero))
        acc = acc + jnp.dot(lhs, d_ref[e], preferred_element_type=jnp.float32)
    o_ref[...] = acc.astype(o_ref.dtype)


def gate_up(route_ids, gathered, paired, tile, sel):
    token_count, width = gathered.shape
    experts, _, paired_width = paired.shape
    steps = token_count // tile // 2
    return pl.pallas_call(
        gate_up_kernel,
        grid_spec=pltpu.PrefetchScalarGridSpec(
            num_scalar_prefetch=1,
            grid=(steps,),
            in_specs=[
                pl.BlockSpec((tile, 2), lambda j, sel_ref: (2 * j + sel_ref[0], 0)),
                pl.BlockSpec((tile, width), lambda j, sel_ref: (2 * j + sel_ref[0], 0)),
                pl.BlockSpec((experts, width, paired_width), lambda j, sel_ref: (0, 0, 0)),
            ],
            out_specs=pl.BlockSpec((2, tile, paired_width), lambda j, sel_ref: (0, j, 0)),
        ),
        out_shape=jax.ShapeDtypeStruct((2, steps * tile, paired_width), jnp.bfloat16),
    )(sel.reshape(1), route_ids, gathered, paired)


def gather_rows(x, axis_name):
    count = lax.axis_size(axis_name)
    copies = jnp.broadcast_to(x[None], (count,) + x.shape)
    received = lax.all_to_all(copies, axis_name, 0, 0, tiled=False)
    return received.reshape((count * x.shape[0],) + x.shape[1:])


def sum_scatter_rows(x, axis_name):
    count = lax.axis_size(axis_name)
    pieces = x.reshape((count, x.shape[0] // count) + x.shape[1:])
    received = lax.all_to_all(pieces, axis_name, 0, 0, tiled=False)
    return jnp.sum(received.astype(jnp.float32), axis=0)


def down(route_ids, hidden_all, down_weight, tile):
    _, token_count, hidden_width = hidden_all.shape
    experts, _, width = down_weight.shape
    return pl.pallas_call(
        down_kernel,
        grid=(token_count // tile,),
        in_specs=[
            pl.BlockSpec((tile, 2), lambda i: (i, 0)),
            pl.BlockSpec((2, tile, hidden_width), lambda i: (0, i, 0)),
            pl.BlockSpec((experts, hidden_width, width), lambda i: (0, 0, 0)),
        ],
        out_specs=pl.BlockSpec((tile, width), lambda i: (i, 0)),
        out_shape=jax.ShapeDtypeStruct((token_count, width), jnp.bfloat16),
    )(route_ids, hidden_all, down_weight)


def col_perm(axis_name, move):
    count = lax.axis_size(axis_name)
    return [(c, move(c)) for c in range(count)]


def x_step(c, step):
    return ((c // 4 + step) % 4) * 4 + c % 4


def pick(chunks, index, axis=0):
    return lax.dynamic_index_in_dim(chunks, index, axis, keepdims=False)


def ring_reduce(chunks, xi, axis_name, direction):
    count = chunks.shape[0]
    perm = col_perm(axis_name, lambda c: x_step(c, direction))
    cur = pick(chunks, (xi - direction) % count)
    for s in range(1, count):
        recv = lax.ppermute(cur, axis_name, perm)
        cur = recv.astype(jnp.float32) + pick(chunks, (xi - direction * (s + 1)) % count).astype(
            jnp.float32
        )
        if s < count - 1:
            cur = cur.astype(chunks.dtype)
    return cur


def ring_gather(block, xi, axis_name, direction, count):
    perm = col_perm(axis_name, lambda c: x_step(c, direction))
    out = jnp.zeros((count,) + block.shape, block.dtype)
    out = lax.dynamic_update_index_in_dim(out, block, xi, 0)
    cur = block
    for s in range(1, count):
        cur = lax.ppermute(cur, axis_name, perm)
        out = lax.dynamic_update_index_in_dim(out, cur, (xi - direction * s) % count, 0)
    return out


def col_reduce_scatter(other, mine, axis_name):
    c = lax.axis_index(axis_name)
    xi, zi = c // 4, (c // 2) % 2
    rows = other.shape[1] // 4
    shape = (4, 2, rows, other.shape[2])
    recv = lax.ppermute(other.reshape(shape), axis_name, col_perm(axis_name, lambda q: q ^ 1))
    core_sum = (mine.reshape(shape).astype(jnp.float32) + recv.astype(jnp.float32)).astype(
        other.dtype
    )
    half = rows // 2
    plus = ring_reduce(core_sum[:, :, :half], xi, axis_name, 1)
    minus = ring_reduce(core_sum[:, :, half:], xi, axis_name, -1)
    x_sum = jnp.concatenate([plus, minus], axis=1)
    recv = lax.ppermute(
        pick(x_sum, 1 - zi).astype(other.dtype), axis_name, col_perm(axis_name, lambda q: q ^ 2)
    )
    return pick(x_sum, zi) + recv.astype(jnp.float32)


def col_all_gather(block, axis_name):
    c = lax.axis_index(axis_name)
    xi, zi, co = c // 4, (c // 2) % 2, c % 2
    recv = lax.ppermute(block, axis_name, col_perm(axis_name, lambda q: q ^ 2))
    z_pair = jnp.where(zi == 0, jnp.stack([block, recv]), jnp.stack([recv, block]))
    half = block.shape[0] // 2
    plus = ring_gather(z_pair[:, :half], xi, axis_name, 1, 4)
    minus = ring_gather(z_pair[:, half:], xi, axis_name, -1, 4)
    x_all = jnp.concatenate([plus, minus], axis=2)
    recv = lax.ppermute(x_all, axis_name, col_perm(axis_name, lambda q: q ^ 1))
    full = jnp.where(co == 0, jnp.stack([x_all, recv], axis=2), jnp.stack([recv, x_all], axis=2))
    return full.reshape((-1,) + block.shape[1:])


def shards(
    tokens,
    gate_weight,
    up_weight,
    down_weight,
    route_ids,
    route_weight,
    prefill_cache,
    dest_col,
    dest_slot,
    pages_used,
):
    decode_cache = move_pages(prefill_cache, dest_col, dest_slot, pages_used)
    gathered = gather_rows(tokens, "row")
    token_count = gathered.shape[0]
    hidden_width = gate_weight.shape[2]
    paired = jnp.concatenate([gate_weight, up_weight], axis=2)
    core = lax.axis_index("col") % 2
    other = gate_up(route_ids, gathered, paired, 256, 1 - core)
    mine = gate_up(route_ids, gathered, paired, 256, core)
    summed = col_reduce_scatter(other, mine, "col")
    share_rows = summed.shape[0]
    own_weight = lax.dynamic_slice_in_dim(
        route_weight.T.reshape(-1), lax.axis_index("col") * share_rows, share_rows, 0
    )
    hidden = (
        own_weight[:, None] * jax.nn.silu(summed[:, :hidden_width]) * summed[:, hidden_width:]
    ).astype(jnp.bfloat16)
    hidden_all = col_all_gather(hidden, "col").reshape(
        2, token_count, hidden_width
    )
    per_token = down(route_ids, hidden_all, down_weight, 256)
    mixed = sum_scatter_rows(per_token, "row").astype(jnp.bfloat16)
    return (mixed, decode_cache)


def solution(mesh):
    in_specs = (
        P("row", "col"),
        P(None, "col", "row"),
        P(None, "col", "row"),
        P(None, "row", "col"),
        P(),
        P(),
        P(None, ("row", "col"), None, None),
        P("row", None, None),
        P("row", None, None),
        P("row", None),
    )
    out_specs = (P("row", "col"), P(None, ("row", "col"), None, None))
    return jax.shard_map(shards, mesh=mesh, in_specs=in_specs, out_specs=out_specs, check_vma=False)
```

```python
import jax
import jax.numpy as jnp
from jax import lax
from jax.sharding import PartitionSpec as P
from jax.experimental import pallas as pl
from jax.experimental.pallas import tpu as pltpu


def move_pages(prefill_cache, dest_col, dest_slot, pages_used):
    col_devices = lax.axis_size("col")
    own_index = lax.axis_index("col")
    slot_count = prefill_cache.shape[1]
    per_peer = slot_count // col_devices
    dest_table = dest_col[0]
    targets = dest_slot[0]
    page_index = jnp.arange(slot_count, dtype=jnp.int32)
    same_dest = dest_table[:, :, None] == dest_table[:, None, :]
    earlier = page_index[None, :] < page_index[:, None]
    dest_rank = jnp.sum((same_dest & earlier[None]).astype(jnp.int32), axis=2)
    send_order = lax.dynamic_index_in_dim(
        dest_table * per_peer + dest_rank, own_index, 0, keepdims=False
    )
    inverse = jnp.zeros((slot_count,), jnp.int32).at[send_order].set(page_index)
    own_used = lax.dynamic_index_in_dim(pages_used[0], own_index, 0, keepdims=False)
    is_live = page_index < own_used
    masked_pages = jnp.where(
        is_live[None, :, None, None], prefill_cache, jnp.zeros((), prefill_cache.dtype)
    )
    received = lax.all_to_all(
        masked_pages[:, inverse], "col", split_axis=1, concat_axis=1, tiled=True
    )
    senders = jnp.arange(col_devices, dtype=jnp.int32)[:, None]
    arrival = jnp.where(dest_table == own_index, senders * per_peer + dest_rank, slot_count)
    slot_of_arrival = (
        jnp.zeros((slot_count + 1,), jnp.int32)
        .at[arrival.reshape(-1)]
        .set(targets.reshape(-1))[:slot_count]
    )
    source_of_slot = jnp.zeros((slot_count,), jnp.int32).at[slot_of_arrival].set(page_index)
    return received[:, source_of_slot]


def gate_up_kernel(sel_ref, ids_ref, x_ref, w_ref, o_ref):
    x = x_ref[...]
    ids = ids_ref[...]
    zero = jnp.zeros_like(x)
    rows = x.shape[0]
    acc = jnp.zeros((2 * rows, w_ref.shape[2]), jnp.float32)
    for e in range(w_ref.shape[0]):
        lhs = jnp.concatenate(
            [jnp.where(ids[:, 0:1] == e, x, zero), jnp.where(ids[:, 1:2] == e, x, zero)], axis=0
        )
        acc = acc + jnp.dot(lhs, w_ref[e], preferred_element_type=jnp.float32)
    o_ref[...] = acc.astype(o_ref.dtype).reshape(o_ref.shape)


def down_kernel(ids_ref, h_ref, d_ref, o_ref):
    ids = ids_ref[...]
    first = h_ref[0]
    second = h_ref[1]
    zero = jnp.zeros_like(first)
    acc = jnp.zeros(o_ref.shape, jnp.float32)
    for e in range(d_ref.shape[0]):
        lhs = jnp.where(ids[:, 0:1] == e, first, jnp.where(ids[:, 1:2] == e, second, zero))
        acc = acc + jnp.dot(lhs, d_ref[e], preferred_element_type=jnp.float32)
    o_ref[...] = acc.astype(o_ref.dtype)


def gate_up(route_ids, gathered, paired, tile, sel):
    token_count, width = gathered.shape
    experts, _, paired_width = paired.shape
    steps = token_count // tile // 2
    return pl.pallas_call(
        gate_up_kernel,
        grid_spec=pltpu.PrefetchScalarGridSpec(
            num_scalar_prefetch=1,
            grid=(steps,),
            in_specs=[
                pl.BlockSpec((tile, 2), lambda j, sel_ref: (2 * j + sel_ref[0], 0)),
                pl.BlockSpec((tile, width), lambda j, sel_ref: (2 * j + sel_ref[0], 0)),
                pl.BlockSpec((experts, width, paired_width), lambda j, sel_ref: (0, 0, 0)),
            ],
            out_specs=pl.BlockSpec((2, tile, paired_width), lambda j, sel_ref: (0, j, 0)),
        ),
        out_shape=jax.ShapeDtypeStruct((2, steps * tile, paired_width), jnp.bfloat16),
    )(sel.reshape(1), route_ids, gathered, paired)


def gather_rows(x, axis_name):
    count = lax.axis_size(axis_name)
    copies = jnp.broadcast_to(x[None], (count,) + x.shape)
    received = lax.all_to_all(copies, axis_name, 0, 0, tiled=False)
    return received.reshape((count * x.shape[0],) + x.shape[1:])


def sum_scatter_rows(x, axis_name):
    count = lax.axis_size(axis_name)
    pieces = x.reshape((count, x.shape[0] // count) + x.shape[1:])
    received = lax.all_to_all(pieces, axis_name, 0, 0, tiled=False)
    return jnp.sum(received.astype(jnp.float32), axis=0)


def down(route_ids, hidden_all, down_weight, tile):
    _, token_count, hidden_width = hidden_all.shape
    experts, _, width = down_weight.shape
    return pl.pallas_call(
        down_kernel,
        grid=(token_count // tile,),
        in_specs=[
            pl.BlockSpec((tile, 2), lambda i: (i, 0)),
            pl.BlockSpec((2, tile, hidden_width), lambda i: (0, i, 0)),
            pl.BlockSpec((experts, hidden_width, width), lambda i: (0, 0, 0)),
        ],
        out_specs=pl.BlockSpec((tile, width), lambda i: (i, 0)),
        out_shape=jax.ShapeDtypeStruct((token_count, width), jnp.bfloat16),
    )(route_ids, hidden_all, down_weight)


def col_perm(axis_name, move):
    count = lax.axis_size(axis_name)
    return [(c, move(c)) for c in range(count)]


def x_step(c, step):
    return ((c // 4 + step) % 4) * 4 + c % 4


def pick(chunks, index, axis=0):
    return lax.dynamic_index_in_dim(chunks, index, axis, keepdims=False)


def ring_reduce(chunks, xi, axis_name, direction, sub):
    count = chunks.shape[0]
    perm = col_perm(axis_name, lambda c: x_step(c, direction))

    def own(index):
        return pick(chunks, index % count)[:, sub]

    cur = own(xi - direction)
    for s in range(1, count):
        recv = lax.ppermute(cur, axis_name, perm)
        cur = recv.astype(jnp.float32) + own(xi - direction * (s + 1)).astype(jnp.float32)
        if s < count - 1:
            cur = cur.astype(chunks.dtype)
    return cur


def ring_gather(block, xi, axis_name, direction, count):
    perm = col_perm(axis_name, lambda c: x_step(c, direction))
    out = jnp.zeros((count,) + block.shape, block.dtype)
    out = lax.dynamic_update_index_in_dim(out, block, xi, 0)
    cur = block
    for s in range(1, count):
        cur = lax.ppermute(cur, axis_name, perm)
        out = lax.dynamic_update_index_in_dim(out, cur, (xi - direction * s) % count, 0)
    return out


def col_reduce_scatter(other, mine, axis_name):
    c = lax.axis_index(axis_name)
    xi, zi = c // 4, (c // 2) % 2
    rows = other.shape[1] // 4
    shape = (4, 2, 2, rows // 2, other.shape[2])
    recv = lax.ppermute(other.reshape(shape), axis_name, col_perm(axis_name, lambda q: q ^ 1))
    core_sum = (mine.reshape(shape).astype(jnp.float32) + recv.astype(jnp.float32)).astype(
        other.dtype
    )
    plus = ring_reduce(core_sum, xi, axis_name, 1, 0)
    minus = ring_reduce(core_sum, xi, axis_name, -1, 1)
    x_sum = jnp.concatenate([plus, minus], axis=1)
    recv = lax.ppermute(
        pick(x_sum, 1 - zi).astype(other.dtype), axis_name, col_perm(axis_name, lambda q: q ^ 2)
    )
    return pick(x_sum, zi) + recv.astype(jnp.float32)


def col_all_gather(block, axis_name):
    c = lax.axis_index(axis_name)
    xi, zi, co = c // 4, (c // 2) % 2, c % 2
    recv = lax.ppermute(block, axis_name, col_perm(axis_name, lambda q: q ^ 2))
    z_pair = jnp.where(zi == 0, jnp.stack([block, recv]), jnp.stack([recv, block]))
    half = block.shape[0] // 2
    plus = ring_gather(z_pair[:, :half], xi, axis_name, 1, 4)
    minus = ring_gather(z_pair[:, half:], xi, axis_name, -1, 4)
    x_all = jnp.concatenate([plus, minus], axis=2)
    recv = lax.ppermute(x_all, axis_name, col_perm(axis_name, lambda q: q ^ 1))
    full = jnp.where(co == 0, jnp.stack([x_all, recv], axis=2), jnp.stack([recv, x_all], axis=2))
    return full.reshape((-1,) + block.shape[1:])


def shards(
    tokens,
    gate_weight,
    up_weight,
    down_weight,
    route_ids,
    route_weight,
    prefill_cache,
    dest_col,
    dest_slot,
    pages_used,
):
    decode_cache = move_pages(prefill_cache, dest_col, dest_slot, pages_used)
    gathered = gather_rows(tokens, "row")
    token_count = gathered.shape[0]
    hidden_width = gate_weight.shape[2]
    experts, width, _ = gate_weight.shape
    padded_width = -(-hidden_width // 128) * 128
    pad = jnp.zeros((experts, width, padded_width - hidden_width), gate_weight.dtype)
    paired = jnp.concatenate([gate_weight, pad, up_weight, pad], axis=2)
    core = lax.axis_index("col") % 2
    other = gate_up(route_ids, gathered, paired, 256, 1 - core)
    mine = gate_up(route_ids, gathered, paired, 256, core)
    summed = col_reduce_scatter(other, mine, "col")
    share_rows = summed.shape[0]
    own_weight = lax.dynamic_slice_in_dim(
        route_weight.T.reshape(-1), lax.axis_index("col") * share_rows, share_rows, 0
    )
    hidden = (
        own_weight[:, None] * jax.nn.silu(summed[:, :padded_width]) * summed[:, padded_width:]
    ).astype(jnp.bfloat16)
    hidden_all = col_all_gather(hidden, "col").reshape(2, token_count, padded_width)
    down_pad = jnp.zeros(
        (experts, padded_width - hidden_width, down_weight.shape[2]), down_weight.dtype
    )
    per_token = down(route_ids, hidden_all, jnp.concatenate([down_weight, down_pad], axis=1), 256)
    mixed = sum_scatter_rows(per_token, "row").astype(jnp.bfloat16)
    return (mixed, decode_cache)


def solution(mesh):
    in_specs = (
        P("row", "col"),
        P(None, "col", "row"),
        P(None, "col", "row"),
        P(None, "row", "col"),
        P(),
        P(),
        P(None, ("row", "col"), None, None),
        P("row", None, None),
        P("row", None, None),
        P("row", None),
    )
    out_specs = (P("row", "col"), P(None, ("row", "col"), None, None))
    return jax.shard_map(shards, mesh=mesh, in_specs=in_specs, out_specs=out_specs, check_vma=False)
```

```python
import jax
import jax.numpy as jnp
from jax import lax
from jax.sharding import PartitionSpec as P
from jax.experimental import pallas as pl
from jax.experimental.pallas import tpu as pltpu


def move_pages(prefill_cache, dest_col, dest_slot, pages_used):
    col_devices = lax.axis_size("col")
    own_index = lax.axis_index("col")
    slot_count = prefill_cache.shape[1]
    per_peer = slot_count // col_devices
    dest_table = dest_col[0]
    targets = dest_slot[0]
    page_index = jnp.arange(slot_count, dtype=jnp.int32)
    same_dest = dest_table[:, :, None] == dest_table[:, None, :]
    earlier = page_index[None, :] < page_index[:, None]
    dest_rank = jnp.sum((same_dest & earlier[None]).astype(jnp.int32), axis=2)
    send_order = lax.dynamic_index_in_dim(
        dest_table * per_peer + dest_rank, own_index, 0, keepdims=False
    )
    inverse = jnp.zeros((slot_count,), jnp.int32).at[send_order].set(page_index)
    own_used = lax.dynamic_index_in_dim(pages_used[0], own_index, 0, keepdims=False)
    is_live = page_index < own_used
    masked_pages = jnp.where(
        is_live[None, :, None, None], prefill_cache, jnp.zeros((), prefill_cache.dtype)
    )[:, inverse]
    received = lax.all_to_all(masked_pages, "col", split_axis=1, concat_axis=1, tiled=True)
    senders = jnp.arange(col_devices, dtype=jnp.int32)[:, None]
    arrival = jnp.where(dest_table == own_index, senders * per_peer + dest_rank, slot_count)
    slot_of_arrival = (
        jnp.zeros((slot_count + 1,), jnp.int32)
        .at[arrival.reshape(-1)]
        .set(targets.reshape(-1))[:slot_count]
    )
    source_of_slot = jnp.zeros((slot_count,), jnp.int32).at[slot_of_arrival].set(page_index)
    return received[:, source_of_slot]


def gate_up_kernel(sel_ref, ids_ref, x_ref, w_ref, o_ref):
    x = x_ref[...]
    ids = ids_ref[...]
    zero = jnp.zeros_like(x)
    rows = x.shape[0]
    acc = jnp.zeros((2 * rows, w_ref.shape[2]), jnp.float32)
    for e in range(w_ref.shape[0]):
        lhs = jnp.concatenate(
            [jnp.where(ids[:, 0:1] == e, x, zero), jnp.where(ids[:, 1:2] == e, x, zero)], axis=0
        )
        acc = acc + jnp.dot(lhs, w_ref[e], preferred_element_type=jnp.float32)
    o_ref[...] = acc.astype(o_ref.dtype).reshape(o_ref.shape)


def down_kernel(ids_ref, h_ref, d_ref, o_ref):
    ids = ids_ref[...]
    first = h_ref[0]
    second = h_ref[1]
    zero = jnp.zeros_like(first)
    acc = jnp.zeros(o_ref.shape, jnp.float32)
    for e in range(d_ref.shape[0]):
        lhs = jnp.where(ids[:, 0:1] == e, first, jnp.where(ids[:, 1:2] == e, second, zero))
        acc = acc + jnp.dot(lhs, d_ref[e], preferred_element_type=jnp.float32)
    o_ref[...] = acc.astype(o_ref.dtype)


def gate_up(route_ids, gathered, paired, tile, sel):
    token_count, width = gathered.shape
    experts, _, paired_width = paired.shape
    steps = token_count // tile // 2
    return pl.pallas_call(
        gate_up_kernel,
        grid_spec=pltpu.PrefetchScalarGridSpec(
            num_scalar_prefetch=1,
            grid=(steps,),
            in_specs=[
                pl.BlockSpec((tile, 2), lambda j, sel_ref: (2 * j + sel_ref[0], 0)),
                pl.BlockSpec((tile, width), lambda j, sel_ref: (2 * j + sel_ref[0], 0)),
                pl.BlockSpec((experts, width, paired_width), lambda j, sel_ref: (0, 0, 0)),
            ],
            out_specs=pl.BlockSpec((2, tile, paired_width), lambda j, sel_ref: (0, j, 0)),
        ),
        out_shape=jax.ShapeDtypeStruct((2, steps * tile, paired_width), jnp.bfloat16),
    )(sel.reshape(1), route_ids, gathered, paired)


def gather_rows(x, axis_name):
    count = lax.axis_size(axis_name)
    copies = jnp.broadcast_to(x[None], (count,) + x.shape)
    received = lax.all_to_all(copies, axis_name, 0, 0, tiled=False)
    return received.reshape((count * x.shape[0],) + x.shape[1:])


def sum_scatter_rows(x, axis_name):
    count = lax.axis_size(axis_name)
    pieces = x.reshape((count, x.shape[0] // count) + x.shape[1:])
    received = lax.all_to_all(pieces, axis_name, 0, 0, tiled=False)
    return jnp.sum(received.astype(jnp.float32), axis=0)


def down(route_ids, hidden_all, down_weight, tile):
    _, token_count, hidden_width = hidden_all.shape
    experts, _, width = down_weight.shape
    return pl.pallas_call(
        down_kernel,
        grid=(token_count // tile,),
        in_specs=[
            pl.BlockSpec((tile, 2), lambda i: (i, 0)),
            pl.BlockSpec((2, tile, hidden_width), lambda i: (0, i, 0)),
            pl.BlockSpec((experts, hidden_width, width), lambda i: (0, 0, 0)),
        ],
        out_specs=pl.BlockSpec((tile, width), lambda i: (i, 0)),
        out_shape=jax.ShapeDtypeStruct((token_count, width), jnp.bfloat16),
    )(route_ids, hidden_all, down_weight)


def col_perm(axis_name, move):
    count = lax.axis_size(axis_name)
    return [(c, move(c)) for c in range(count)]


def x_step(c, step):
    return ((c // 4 + step) % 4) * 4 + c % 4


def pick(chunks, index, axis=0):
    return lax.dynamic_index_in_dim(chunks, index, axis, keepdims=False)


def ring_reduce(chunks, xi, axis_name, direction, sub):
    count = chunks.shape[0]
    perm = col_perm(axis_name, lambda c: x_step(c, direction))

    def own(index):
        return pick(chunks, index % count)[:, sub]

    cur = own(xi - direction)
    for s in range(1, count):
        recv = lax.ppermute(cur, axis_name, perm)
        cur = recv.astype(jnp.float32) + own(xi - direction * (s + 1)).astype(jnp.float32)
        if s < count - 1:
            cur = cur.astype(chunks.dtype)
    return cur


def ring_gather(block, xi, axis_name, direction, count):
    perm = col_perm(axis_name, lambda c: x_step(c, direction))
    out = jnp.zeros((count,) + block.shape, block.dtype)
    out = lax.dynamic_update_index_in_dim(out, block, xi, 0)
    cur = block
    for s in range(1, count):
        cur = lax.ppermute(cur, axis_name, perm)
        out = lax.dynamic_update_index_in_dim(out, cur, (xi - direction * s) % count, 0)
    return out


def col_reduce_scatter(other, mine, axis_name):
    c = lax.axis_index(axis_name)
    xi, zi = c // 4, (c // 2) % 2
    rows = other.shape[1] // 4
    shape = (4, 2, 2, rows // 2, other.shape[2])
    recv = lax.ppermute(other.reshape(shape), axis_name, col_perm(axis_name, lambda q: q ^ 1))
    core_sum = (mine.reshape(shape).astype(jnp.float32) + recv.astype(jnp.float32)).astype(
        other.dtype
    )
    plus = ring_reduce(core_sum, xi, axis_name, 1, 0)
    minus = ring_reduce(core_sum, xi, axis_name, -1, 1)
    x_sum = jnp.concatenate([plus, minus], axis=1)
    recv = lax.ppermute(
        pick(x_sum, 1 - zi).astype(other.dtype), axis_name, col_perm(axis_name, lambda q: q ^ 2)
    )
    return pick(x_sum, zi) + recv.astype(jnp.float32)


def col_all_gather(block, axis_name):
    c = lax.axis_index(axis_name)
    xi, zi, co = c // 4, (c // 2) % 2, c % 2
    recv = lax.ppermute(block, axis_name, col_perm(axis_name, lambda q: q ^ 2))
    z_pair = jnp.where(zi == 0, jnp.stack([block, recv]), jnp.stack([recv, block]))
    half = block.shape[0] // 2
    plus = ring_gather(z_pair[:, :half], xi, axis_name, 1, 4)
    minus = ring_gather(z_pair[:, half:], xi, axis_name, -1, 4)
    x_all = jnp.concatenate([plus, minus], axis=2)
    recv = lax.ppermute(x_all, axis_name, col_perm(axis_name, lambda q: q ^ 1))
    full = jnp.where(co == 0, jnp.stack([x_all, recv], axis=2), jnp.stack([recv, x_all], axis=2))
    return full.reshape((-1,) + block.shape[1:])


def shards(
    tokens,
    gate_weight,
    up_weight,
    down_weight,
    route_ids,
    route_weight,
    prefill_cache,
    dest_col,
    dest_slot,
    pages_used,
):
    decode_cache = move_pages(prefill_cache, dest_col, dest_slot, pages_used)
    gathered = gather_rows(tokens, "row")
    token_count = gathered.shape[0]
    hidden_width = gate_weight.shape[2]
    experts, width, _ = gate_weight.shape
    padded_width = -(-hidden_width // 128) * 128
    pad = jnp.zeros((experts, width, padded_width - hidden_width), gate_weight.dtype)
    paired = jnp.concatenate([gate_weight, pad, up_weight, pad], axis=2)
    core = lax.axis_index("col") % 2
    other = gate_up(route_ids, gathered, paired, 256, 1 - core)
    mine = gate_up(route_ids, gathered, paired, 256, core)
    summed = col_reduce_scatter(other, mine, "col")
    share_rows = summed.shape[0]
    own_weight = lax.dynamic_slice_in_dim(
        route_weight.T.reshape(-1), lax.axis_index("col") * share_rows, share_rows, 0
    )
    hidden = (
        own_weight[:, None] * jax.nn.silu(summed[:, :padded_width]) * summed[:, padded_width:]
    ).astype(jnp.bfloat16)
    hidden_all = col_all_gather(hidden, "col").reshape(2, token_count, padded_width)
    down_pad = jnp.zeros(
        (experts, padded_width - hidden_width, down_weight.shape[2]), down_weight.dtype
    )
    per_token = down(route_ids, hidden_all, jnp.concatenate([down_weight, down_pad], axis=1), 1024)
    mixed = sum_scatter_rows(per_token, "row").astype(jnp.bfloat16)
    return (mixed, decode_cache)


def solution(mesh):
    in_specs = (
        P("row", "col"),
        P(None, "col", "row"),
        P(None, "col", "row"),
        P(None, "row", "col"),
        P(),
        P(),
        P(None, ("row", "col"), None, None),
        P("row", None, None),
        P("row", None, None),
        P("row", None),
    )
    out_specs = (P("row", "col"), P(None, ("row", "col"), None, None))
    return jax.shard_map(shards, mesh=mesh, in_specs=in_specs, out_specs=out_specs, check_vma=False)
```
